32 devices in a mesh: tile: 8 (over z, x), rows: 4 (over y, core).
Axes of the slice: x: 2, y: 2, z: 4, core: 2. Of those that a mesh axis runs over, the one named last changes fastest.
Arguments:
- adjoint_rows: bfloat16 [2048, 128, 128], P('rows', 'tile'), may hold values from -6 to 6
- panel_index: int32 [2, 64], P(None, 'rows'), may hold values from 0 to 511
- coef_class: int32 [8], P('tile'), may hold values from 0 to 7
- class_gain: float32 [8], replicated, may hold values from 0.25 to 1
- cell_coef: float32 [128, 128], P('tile'), may hold values from 0.3 to 1
Outputs:
- hessian: float32 [2, 64, 2048], P(None, 'tile', 'rows')
The draws below stay inside these ranges and needn't reach their ends.
Inputs may be any that keep to these rules, and one draw needn't show every extreme that they name: `panel_index`: panel row j is taken from row block j // 16; the entry is its offset in that block.
All inputs are finite; a program needn't handle non-finite values.
Results may differ from the reference program's by a relative error of at most 0.00081.
Values may be sent and summed in bfloat16 or wider, within the bound.
No kernel may reach another device: no remote copies, remote signals or barrier semaphores. Data moves between devices by JAX's collectives and lax.ppermute only.
A program may use at most 64 MiB of HBM per device.

```python
import math
import jax
import jax.numpy as jnp
from jax import lax

TA = 16
NB = 128
R_DEV = 512
PANEL_DEV = 16
PANELS = 2
SMOOTH = 4
NCLASS = 8
TILES = 8
PA = 128
ROWS_TOTAL = 2048
PANEL = 64


def place_ends(values, own_key, low, largest):
    extent = values.shape
    spot = [jax.random.randint(jax.random.fold_in(own_key, axis), (), 0, extent[axis]) for axis in range(len(extent))]
    values = values.at[tuple(spot)].set(low)
    longest = extent.index(max(extent))
    spot[longest] = (spot[longest] + 1) % extent[longest]
    return values.at[tuple(spot)].set(largest)


def shard_levels(key, shape, split, smallest, largest):
    def one(dim, parts):
        steps = jax.random.uniform(jax.random.fold_in(jax.random.fold_in(key, 6), dim), (parts,), jnp.float32, smallest / len(split), largest / len(split))
        return jnp.repeat(jnp.exp(steps), shape[dim] // parts).reshape((-1,) + (1,) * (len(shape) - dim - 1))

    level = one(*split[0])
    for cut in split[1:]:
        level = level * one(*cut)
    return level


def scatter_about(own_key, dims, deviation, most, shards=(), held_as=jnp.bfloat16):
    drawn = deviation * jax.random.normal(own_key, dims, jnp.float32)
    if shards:
        drawn = drawn * shard_levels(own_key, dims, shards, -0.22, 0.18)
    return jnp.clip(drawn, -most, most).astype(held_as)


def setup_inputs(seed: int = 0) -> dict:
    splits = jax.random.split(jax.random.key(seed), 6)
    return {
        "adjoint_rows": scatter_about(splits[0], (ROWS_TOTAL, PA, NB), 1.0, 6.0, ((0, 4), (1, 8))),
        "panel_index": place_ends(jax.random.randint(splits[1], (PANELS, PANEL), 0, R_DEV), jax.random.fold_in(splits[1], 1), 0, R_DEV - 1).astype(jnp.int32),
        "coef_class": place_ends(jax.random.randint(splits[2], (TILES,), 0, NCLASS), jax.random.fold_in(splits[2], 1), 0, NCLASS - 1).astype(jnp.int32),
        "class_gain": jnp.clip(jnp.exp(jax.random.uniform(splits[3], (NCLASS,), jnp.float32, math.log(0.25), math.log(1.0))), 0.25, 1.0),
        "cell_coef": jnp.clip(jnp.exp(math.log(1.0) - 1.2039728 * jax.random.uniform(splits[4], (PA, NB), jnp.float32) ** shard_levels(splits[4], (PA, NB), ((0, 8),), -0.2, 0.2)), 0.3, 1.0),
    }


def step_core(padded, coef_pad):
    middle = padded[..., 1:-1, :]
    coef_mid = coef_pad[1:-1, :]
    face_up = 0.5 * (coef_pad[:-2, :] + coef_mid)
    face_down = 0.5 * (coef_pad[2:, :] + coef_mid)
    side_vals = jnp.pad(middle, [(0, 0)] * (middle.ndim - 1) + [(1, 1)])
    side_coef = jnp.pad(coef_mid, ((0, 0), (1, 1)))
    face_left = 0.5 * (side_coef[:, :-2] + coef_mid)
    face_right = 0.5 * (side_coef[:, 2:] + coef_mid)
    result = middle + face_up * (padded[..., :-2, :] - middle)
    result = result + face_down * (padded[..., 2:, :] - middle)
    result = result + face_left * (side_vals[..., :-2] - middle)
    return result + face_right * (side_vals[..., 2:] - middle)

def reference(adjoint_rows, panel_index, coef_class, class_gain, cell_coef):
    rows_total = adjoint_rows.shape[0]
    blocks = (jnp.arange(PANEL, dtype=jnp.int32) // PANEL_DEV * R_DEV).astype(jnp.int32)
    global_index = (panel_index + blocks[None, :]).astype(jnp.int32)
    tile_gain = jnp.repeat(0.2 * class_gain[coef_class], TA)[:, None]
    diffusivity = tile_gain * cell_coef
    coef_pad = jnp.pad(diffusivity, ((1, 1), (0, 0)))
    flat_rows = adjoint_rows.reshape(rows_total, PA * NB)
    gram_scale = 1.0 / math.sqrt(PA * NB)

    def one_panel(index_row):
        state = adjoint_rows[index_row].astype(jnp.float32)
        for sweep_no in range(SMOOTH):
            state = step_core(jnp.pad(state, ((0, 0), (1, 1), (0, 0))), coef_pad)
        smoothed = state.astype(jnp.bfloat16).reshape(PANEL, PA * NB)
        product = lax.dot_general(smoothed, flat_rows, (((1,), (1,)), ((), ())), preferred_element_type=jnp.float32)
        return product * gram_scale
    return lax.map(one_panel, global_index)
```

```python
import math

import jax
import jax.numpy as jnp
from jax import lax
from jax.sharding import PartitionSpec as P

SMOOTH = 4


def halo_exchange(block, width):
    count = lax.axis_size("tile")
    head = lax.slice_in_dim(block, 0, width, axis=1)
    tail = lax.slice_in_dim(block, block.shape[1] - width, block.shape[1], axis=1)
    from_below = lax.ppermute(tail, "tile", [(i, i + 1) for i in range(count - 1)])
    from_above = lax.ppermute(head, "tile", [(i + 1, i) for i in range(count - 1)])
    return jnp.concatenate([from_below, block, from_above], axis=1)


def step_core(padded, coef_pad):
    middle = padded[..., 1:-1, :]
    coef_mid = coef_pad[1:-1, :]
    face_up = 0.5 * (coef_pad[:-2, :] + coef_mid)
    face_down = 0.5 * (coef_pad[2:, :] + coef_mid)
    side_vals = jnp.pad(middle, [(0, 0)] * (middle.ndim - 1) + [(1, 1)])
    side_coef = jnp.pad(coef_mid, ((0, 0), (1, 1)))
    face_left = 0.5 * (side_coef[:, :-2] + coef_mid)
    face_right = 0.5 * (side_coef[:, 2:] + coef_mid)
    result = middle + face_up * (padded[..., :-2, :] - middle)
    result = result + face_down * (padded[..., 2:, :] - middle)
    result = result + face_left * (side_vals[..., :-2] - middle)
    return result + face_right * (side_vals[..., 2:] - middle)


def per_device(adjoint_rows, panel_index, coef_class, class_gain, cell_coef):
    resident = adjoint_rows.shape[0]
    lines = cell_coef.shape[0]
    cells = cell_coef.shape[1]
    panel_count = panel_index.shape[0]
    per_block = panel_index.shape[1]
    tiles = lax.axis_size("tile")
    halo = SMOOTH
    assert lines >= halo
    classes = jnp.arange(class_gain.shape[0], dtype=jnp.int32)
    own_gain = jnp.sum(jnp.where(classes == coef_class[0], class_gain, 0.0))
    diffusivity = 0.2 * own_gain * cell_coef
    picked = jnp.take(adjoint_rows, panel_index.reshape(-1), axis=0)
    picked = picked.astype(jnp.float32)
    stacked = jnp.concatenate([picked, diffusivity[None]], axis=0)
    wide = halo_exchange(stacked, halo)
    state = wide[:-1]
    coef_wide = wide[-1]
    ext = lines + 2 * halo
    first = lax.axis_index("tile") * lines - halo
    line_no = first + lax.broadcasted_iota(jnp.int32, (ext, 1), 0)
    inside = (line_no >= 0) & (line_no < tiles * lines)
    coef_pad = jnp.pad(coef_wide, ((1, 1), (0, 0)))
    for sweep_no in range(SMOOTH):
        padded = jnp.pad(state, ((0, 0), (1, 1), (0, 0)))
        state = jnp.where(inside[None], step_core(padded, coef_pad), 0.0)
    state = state[:, halo : halo + lines]
    smoothed = state.astype(jnp.bfloat16).reshape(panel_count, per_block, lines, cells)
    flat_rows = adjoint_rows.reshape(resident, lines * cells)
    gram_scale = 1.0 / math.sqrt(tiles * lines * cells)
    rows_piece = lax.all_gather(smoothed, "rows", axis=1, tiled=True)
    panel = rows_piece.shape[1]
    flat_piece = rows_piece.reshape(-1, lines * cells)
    product = lax.dot_general(
        flat_piece, flat_rows, (((1,), (1,)), ((), ())), preferred_element_type=jnp.float32
    )
    terms = (product * gram_scale).reshape(panel_count, tiles, panel // tiles, resident)
    terms = terms.transpose(1, 0, 2, 3)
    parts = lax.all_to_all(terms, "tile", 0, 0, tiled=True)
    return jnp.sum(parts, axis=0)


def solution(mesh):
    return jax.shard_map(
        per_device,
        mesh=mesh,
        in_specs=(P("rows", "tile", None), P(None, "rows"), P("tile"), P(), P("tile", None)),
        out_specs=P(None, "tile", "rows"),
        check_vma=False,
    )
```

```python
import math

import jax
import jax.numpy as jnp
from jax import lax
from jax.sharding import PartitionSpec as P

SMOOTH = 4


def step_core(padded, coef_pad):
    middle = padded[..., 1:-1, :]
    coef_mid = coef_pad[1:-1, :]
    face_up = 0.5 * (coef_pad[:-2, :] + coef_mid)
    face_down = 0.5 * (coef_pad[2:, :] + coef_mid)
    side_vals = jnp.pad(middle, [(0, 0)] * (middle.ndim - 1) + [(1, 1)])
    side_coef = jnp.pad(coef_mid, ((0, 0), (1, 1)))
    face_left = 0.5 * (side_coef[:, :-2] + coef_mid)
    face_right = 0.5 * (side_coef[:, 2:] + coef_mid)
    result = middle + face_up * (padded[..., :-2, :] - middle)
    result = result + face_down * (padded[..., 2:, :] - middle)
    result = result + face_left * (side_vals[..., :-2] - middle)
    return result + face_right * (side_vals[..., 2:] - middle)


def per_device(adjoint_rows, panel_index, coef_class, class_gain, cell_coef):
    resident = adjoint_rows.shape[0]
    lines = cell_coef.shape[0]
    cells = cell_coef.shape[1]
    panel_count = panel_index.shape[0]
    per_block = panel_index.shape[1]
    tiles = lax.axis_size("tile")
    halo = SMOOTH
    assert lines >= halo
    lo_rows = adjoint_rows[:, :halo].at[panel_index].get(mode="promise_in_bounds")
    hi_rows = adjoint_rows[:, lines - halo :].at[panel_index].get(mode="promise_in_bounds")
    own_class = jnp.broadcast_to(coef_class.astype(jnp.float32).reshape(1, 1, 1), (1, halo, cells))

    def edge(rows, coef):
        flat = rows.reshape(-1, halo, cells).astype(jnp.float32)
        return jnp.concatenate([flat, coef[None], own_class], axis=0)

    count = lax.axis_size("tile")
    from_below = lax.ppermute(edge(hi_rows, cell_coef[lines - halo :]), "tile", [(i, i + 1) for i in range(count - 1)])
    from_above = lax.ppermute(edge(lo_rows, cell_coef[:halo]), "tile", [(i + 1, i) for i in range(count - 1)])

    def diffusion(raw_coef, class_code):
        gain = class_gain[class_code]
        return 0.2 * gain * raw_coef

    diffusivity = diffusion(cell_coef, coef_class[0])
    picked = adjoint_rows.at[panel_index].get(mode="promise_in_bounds")
    picked = picked.reshape(-1, lines, cells).astype(jnp.float32)
    state = jnp.concatenate([from_below[:-2], picked, from_above[:-2]], axis=1)
    coef_wide = jnp.concatenate(
        [
            diffusion(from_below[-2], from_below[-1, 0, 0].astype(jnp.int32)),
            diffusivity,
            diffusion(from_above[-2], from_above[-1, 0, 0].astype(jnp.int32)),
        ],
        axis=0,
    )
    ext = lines + 2 * halo
    first = lax.axis_index("tile") * lines - halo
    line_no = first + lax.broadcasted_iota(jnp.int32, (ext, 1), 0)
    inside = (line_no >= 0) & (line_no < tiles * lines)
    coef_pad = jnp.pad(coef_wide, ((1, 1), (0, 0)))
    for sweep_no in range(SMOOTH):
        padded = jnp.pad(state, ((0, 0), (1, 1), (0, 0)))
        state = jnp.where(inside[None], step_core(padded, coef_pad), 0.0)
    state = state[:, halo : halo + lines]
    smoothed = state.astype(jnp.bfloat16).reshape(panel_count, per_block, lines, cells)
    flat_rows = adjoint_rows.reshape(resident, lines * cells)
    gram_scale = 1.0 / math.sqrt(tiles * lines * cells)
    rows_piece = lax.all_gather(smoothed, "rows", axis=1, tiled=True)
    panel = rows_piece.shape[1]
    flat_piece = rows_piece.reshape(-1, lines * cells)
    product = lax.dot_general(
        flat_piece, flat_rows, (((1,), (1,)), ((), ())), preferred_element_type=jnp.float32
    )
    terms = (product * gram_scale).reshape(panel_count, tiles, panel // tiles, resident)
    terms = terms.transpose(1, 0, 2, 3)
    parts = lax.all_to_all(terms, "tile", 0, 0, tiled=True)
    return jnp.sum(parts, axis=0)


def solution(mesh):
    return jax.shard_map(
        per_device,
        mesh=mesh,
        in_specs=(P("rows", "tile", None), P(None, "rows"), P("tile"), P(), P("tile", None)),
        out_specs=P(None, "tile", "rows"),
        check_vma=False,
    )
```

```python
import math

import jax
import jax.numpy as jnp
from jax import lax
from jax.sharding import PartitionSpec as P

SMOOTH = 4


def step_core(padded, coef_pad):
    middle = padded[..., 1:-1, :]
    coef_mid = coef_pad[1:-1, :]
    face_up = 0.5 * (coef_pad[:-2, :] + coef_mid)
    face_down = 0.5 * (coef_pad[2:, :] + coef_mid)
    side_vals = jnp.pad(middle, [(0, 0)] * (middle.ndim - 1) + [(1, 1)])
    side_coef = jnp.pad(coef_mid, ((0, 0), (1, 1)))
    face_left = 0.5 * (side_coef[:, :-2] + coef_mid)
    face_right = 0.5 * (side_coef[:, 2:] + coef_mid)
    result = middle + face_up * (padded[..., :-2, :] - middle)
    result = result + face_down * (padded[..., 2:, :] - middle)
    result = result + face_left * (side_vals[..., :-2] - middle)
    return result + face_right * (side_vals[..., 2:] - middle)


def per_device(adjoint_rows, panel_index, coef_class, class_gain, cell_coef):
    resident = adjoint_rows.shape[0]
    lines = cell_coef.shape[0]
    cells = cell_coef.shape[1]
    panel_count = panel_index.shape[0]
    per_block = panel_index.shape[1]
    tiles = lax.axis_size("tile")
    halo = SMOOTH
    assert lines >= halo
    picked = lax.gather(
        adjoint_rows,
        panel_index[..., None],
        lax.GatherDimensionNumbers(offset_dims=(2, 3), collapsed_slice_dims=(0,), start_index_map=(0,)),
        (1, lines, cells),
        mode=lax.GatherScatterMode.PROMISE_IN_BOUNDS,
    )
    picked = picked.reshape(-1, lines, cells).astype(jnp.float32)
    edge_rows = jnp.concatenate([picked[:, :halo], picked[:, lines - halo :]], axis=0)
    flat_index = panel_index.reshape(-1, 1)
    picks = flat_index.shape[0]
    own_class = jnp.broadcast_to(coef_class.astype(jnp.float32).reshape(1, 1, 1), (1, halo, cells))

    def edge(rows, coef):
        return jnp.concatenate([rows, coef[None], own_class], axis=0)

    count = lax.axis_size("tile")
    from_below = lax.ppermute(
        edge(edge_rows[picks:], cell_coef[lines - halo :]), "tile", [(i, i + 1) for i in range(count - 1)]
    )
    from_above = lax.ppermute(edge(edge_rows[:picks], cell_coef[:halo]), "tile", [(i + 1, i) for i in range(count - 1)])
    classes = lax.broadcasted_iota(jnp.int32, (class_gain.shape[0], 1, 1), 0).astype(jnp.float32)

    def diffusion(raw_coef, class_code):
        gain = jnp.sum(jnp.where(classes == class_code[None], class_gain[:, None, None], 0.0), axis=0)
        return 0.2 * gain * raw_coef

    diffusivity = diffusion(cell_coef, jnp.broadcast_to(coef_class.astype(jnp.float32)[:, None], cell_coef.shape))
    state = jnp.concatenate([from_below[:-2], picked, from_above[:-2]], axis=1)
    coef_wide = jnp.concatenate(
        [diffusion(from_below[-2], from_below[-1]), diffusivity, diffusion(from_above[-2], from_above[-1])], axis=0
    )
    ext = lines + 2 * halo
    first = lax.axis_index("tile") * lines - halo
    line_no = first + lax.broadcasted_iota(jnp.int32, (ext, 1), 0)
    inside = (line_no >= 0) & (line_no < tiles * lines)
    coef_pad = jnp.pad(coef_wide, ((1, 1), (0, 0)))
    for sweep_no in range(SMOOTH):
        padded = jnp.pad(state, ((0, 0), (1, 1), (0, 0)))
        state = jnp.where(inside[None], step_core(padded, coef_pad), 0.0)
    state = state[:, halo : halo + lines]
    smoothed = state.astype(jnp.bfloat16).reshape(panel_count, per_block, lines, cells)
    flat_rows = adjoint_rows.reshape(resident, lines * cells)
    gram_scale = 1.0 / math.sqrt(tiles * lines * cells)
    rows_piece = lax.all_gather(smoothed, "rows", axis=1, tiled=True)
    panel = rows_piece.shape[1]
    flat_piece = rows_piece.reshape(-1, lines * cells)
    product = lax.dot_general(
        flat_piece, flat_rows, (((1,), (1,)), ((), ())), preferred_element_type=jnp.float32
    )
    terms = (product * gram_scale).reshape(panel_count, tiles, panel // tiles, resident)
    terms = terms.transpose(1, 0, 2, 3)
    parts = lax.all_to_all(terms, "tile", 0, 0, tiled=True)
    return jnp.sum(parts, axis=0)


def solution(mesh):
    return jax.shard_map(
        per_device,
        mesh=mesh,
        in_specs=(P("rows", "tile", None), P(None, "rows"), P("tile"), P(), P("tile", None)),
        out_specs=P(None, "tile", "rows"),
        check_vma=False,
    )
```

```python
import functools
import math

import jax
import jax.numpy as jnp
from jax import lax
from jax.experimental import pallas as pl
from jax.experimental.pallas import tpu as pltpu
from jax.sharding import PartitionSpec as P

SMOOTH = 4


def gather_kernel(halo, index_ref, class_ref, rows_hbm, coef_ref, picked_ref, down_ref, up_ref, buf, sems):
    panels, per_block = index_ref.shape
    count = panels * per_block
    lines = buf.shape[1]
    copies = []
    for i in range(count):
        copy = pltpu.make_async_copy(rows_hbm.at[index_ref[i // per_block, i % per_block]], buf.at[i], sems.at[i])
        copy.start()
        copies.append(copy)
    for copy in copies:
        copy.wait()
    rows = buf[...].astype(jnp.float32)
    picked_ref[...] = rows
    code = jnp.full(down_ref.shape[1:], class_ref[0].astype(jnp.float32), jnp.float32)
    down_ref[:count] = rows[:, :halo]
    down_ref[count] = coef_ref[:halo]
    down_ref[count + 1] = code
    up_ref[:count] = rows[:, lines - halo :]
    up_ref[count] = coef_ref[lines - halo :]
    up_ref[count + 1] = code


def gather_rows(adjoint_rows, panel_index, coef_class, cell_coef, halo):
    count = panel_index.size
    lines, cells = cell_coef.shape
    edge = jax.ShapeDtypeStruct((count + 2, halo, cells), jnp.float32)
    smem = pl.BlockSpec(memory_space=pltpu.SMEM)
    vmem = pl.BlockSpec(memory_space=pltpu.VMEM)
    return pl.pallas_call(
        functools.partial(gather_kernel, halo),
        out_shape=(jax.ShapeDtypeStruct((count, lines, cells), jnp.float32), edge, edge),
        in_specs=[smem, smem, pl.BlockSpec(memory_space=pl.ANY), vmem],
        out_specs=(vmem, vmem, vmem),
        scratch_shapes=[pltpu.VMEM((count, lines, cells), adjoint_rows.dtype), pltpu.SemaphoreType.DMA((count,))],
        cost_estimate=pl.CostEstimate(flops=0, transcendentals=0, bytes_accessed=count * lines * cells * 6),
    )(panel_index, coef_class, adjoint_rows, cell_coef)


def step_core(padded, coef_pad):
    middle = padded[..., 1:-1, :]
    coef_mid = coef_pad[1:-1, :]
    face_up = 0.5 * (coef_pad[:-2, :] + coef_mid)
    face_down = 0.5 * (coef_pad[2:, :] + coef_mid)
    side_vals = jnp.pad(middle, [(0, 0)] * (middle.ndim - 1) + [(1, 1)])
    side_coef = jnp.pad(coef_mid, ((0, 0), (1, 1)))
    face_left = 0.5 * (side_coef[:, :-2] + coef_mid)
    face_right = 0.5 * (side_coef[:, 2:] + coef_mid)
    result = middle + face_up * (padded[..., :-2, :] - middle)
    result = result + face_down * (padded[..., 2:, :] - middle)
    result = result + face_left * (side_vals[..., :-2] - middle)
    return result + face_right * (side_vals[..., 2:] - middle)


def per_device(adjoint_rows, panel_index, coef_class, class_gain, cell_coef):
    resident = adjoint_rows.shape[0]
    lines = cell_coef.shape[0]
    cells = cell_coef.shape[1]
    panel_count = panel_index.shape[0]
    per_block = panel_index.shape[1]
    tiles = lax.axis_size("tile")
    halo = SMOOTH
    assert lines >= halo
    picked, down_edge, up_edge = gather_rows(adjoint_rows, panel_index, coef_class, cell_coef, halo)
    count = lax.axis_size("tile")
    from_below = lax.ppermute(up_edge, "tile", [(i, i + 1) for i in range(count - 1)])
    from_above = lax.ppermute(down_edge, "tile", [(i + 1, i) for i in range(count - 1)])
    classes = lax.broadcasted_iota(jnp.int32, (class_gain.shape[0], 1, 1), 0).astype(jnp.float32)

    def diffusion(raw_coef, class_code):
        gain = jnp.sum(jnp.where(classes == class_code[None], class_gain[:, None, None], 0.0), axis=0)
        return 0.2 * gain * raw_coef

    diffusivity = diffusion(cell_coef, jnp.broadcast_to(coef_class.astype(jnp.float32)[:, None], cell_coef.shape))
    state = jnp.concatenate([from_below[:-2], picked, from_above[:-2]], axis=1)
    coef_wide = jnp.concatenate(
        [diffusion(from_below[-2], from_below[-1]), diffusivity, diffusion(from_above[-2], from_above[-1])], axis=0
    )
    ext = lines + 2 * halo
    first = lax.axis_index("tile") * lines - halo
    line_no = first + lax.broadcasted_iota(jnp.int32, (ext, 1), 0)
    inside = (line_no >= 0) & (line_no < tiles * lines)
    coef_pad = jnp.pad(coef_wide, ((1, 1), (0, 0)))
    for sweep_no in range(SMOOTH):
        padded = jnp.pad(state, ((0, 0), (1, 1), (0, 0)))
        state = jnp.where(inside[None], step_core(padded, coef_pad), 0.0)
    state = state[:, halo : halo + lines]
    smoothed = state.astype(jnp.bfloat16).reshape(panel_count, per_block, lines, cells)
    flat_rows = adjoint_rows.reshape(resident, lines * cells)
    gram_scale = 1.0 / math.sqrt(tiles * lines * cells)
    rows_piece = lax.all_gather(smoothed, "rows", axis=1, tiled=True)
    panel = rows_piece.shape[1]
    flat_piece = rows_piece.reshape(-1, lines * cells)
    product = lax.dot_general(
        flat_piece, flat_rows, (((1,), (1,)), ((), ())), preferred_element_type=jnp.float32
    )
    terms = (product * gram_scale).reshape(panel_count, tiles, panel // tiles, resident)
    terms = terms.transpose(1, 0, 2, 3)
    parts = lax.all_to_all(terms, "tile", 0, 0, tiled=True)
    return jnp.sum(parts, axis=0)


def solution(mesh):
    return jax.shard_map(
        per_device,
        mesh=mesh,
        in_specs=(P("rows", "tile", None), P(None, "rows"), P("tile"), P(), P("tile", None)),
        out_specs=P(None, "tile", "rows"),
        check_vma=False,
    )
```

```python
import functools
import math

import jax
import jax.numpy as jnp
from jax import lax
from jax.experimental import pallas as pl
from jax.experimental.pallas import tpu as pltpu
from jax.sharding import PartitionSpec as P

SMOOTH = 4


def gather_kernel(halo, index_ref, class_ref, rows_hbm, coef_ref, picked_ref, down_ref, up_ref, buf, sems):
    panels, per_block = index_ref.shape
    count = panels * per_block
    lines = buf.shape[1]
    copies = []
    for i in range(count):
        copy = pltpu.make_async_copy(rows_hbm.at[index_ref[i // per_block, i % per_block]], buf.at[i], sems.at[i])
        copy.start()
        copies.append(copy)
    for copy in copies:
        copy.wait()
    picked_ref[...] = buf[...]
    rows = buf[...].astype(jnp.float32)
    code = jnp.full(down_ref.shape[1:], class_ref[0].astype(jnp.float32), jnp.float32)
    down_ref[:count] = rows[:, :halo]
    down_ref[count] = coef_ref[:halo]
    down_ref[count + 1] = code
    up_ref[:count] = rows[:, lines - halo :]
    up_ref[count] = coef_ref[lines - halo :]
    up_ref[count + 1] = code


def gather_rows(adjoint_rows, panel_index, coef_class, cell_coef, halo):
    count = panel_index.size
    lines, cells = cell_coef.shape
    edge = jax.ShapeDtypeStruct((count + 2, halo, cells), jnp.float32)
    smem = pl.BlockSpec(memory_space=pltpu.SMEM)
    vmem = pl.BlockSpec(memory_space=pltpu.VMEM)
    return pl.pallas_call(
        functools.partial(gather_kernel, halo),
        out_shape=(jax.ShapeDtypeStruct((count, lines, cells), adjoint_rows.dtype), edge, edge),
        in_specs=[smem, smem, pl.BlockSpec(memory_space=pl.ANY), vmem],
        out_specs=(vmem, vmem, vmem),
        scratch_shapes=[pltpu.VMEM((count, lines, cells), adjoint_rows.dtype), pltpu.SemaphoreType.DMA((count,))],
        cost_estimate=pl.CostEstimate(flops=0, transcendentals=0, bytes_accessed=count * lines * cells * 6),
    )(panel_index, coef_class, adjoint_rows, cell_coef)


def step_core(padded, coef_pad):
    middle = padded[..., 1:-1, :]
    coef_mid = coef_pad[1:-1, :]
    face_up = 0.5 * (coef_pad[:-2, :] + coef_mid)
    face_down = 0.5 * (coef_pad[2:, :] + coef_mid)
    side_vals = jnp.pad(middle, [(0, 0)] * (middle.ndim - 1) + [(1, 1)])
    side_coef = jnp.pad(coef_mid, ((0, 0), (1, 1)))
    face_left = 0.5 * (side_coef[:, :-2] + coef_mid)
    face_right = 0.5 * (side_coef[:, 2:] + coef_mid)
    result = middle + face_up * (padded[..., :-2, :] - middle)
    result = result + face_down * (padded[..., 2:, :] - middle)
    result = result + face_left * (side_vals[..., :-2] - middle)
    return result + face_right * (side_vals[..., 2:] - middle)


def per_device(adjoint_rows, panel_index, coef_class, class_gain, cell_coef):
    resident = adjoint_rows.shape[0]
    lines = cell_coef.shape[0]
    cells = cell_coef.shape[1]
    panel_count = panel_index.shape[0]
    per_block = panel_index.shape[1]
    tiles = lax.axis_size("tile")
    halo = SMOOTH
    assert lines >= halo
    picked, down_edge, up_edge = gather_rows(adjoint_rows, panel_index, coef_class, cell_coef, halo)
    count = lax.axis_size("tile")
    from_below = lax.ppermute(up_edge, "tile", [(i, i + 1) for i in range(count - 1)])
    from_above = lax.ppermute(down_edge, "tile", [(i + 1, i) for i in range(count - 1)])
    classes = lax.broadcasted_iota(jnp.int32, (class_gain.shape[0], 1, 1), 0).astype(jnp.float32)

    def diffusion(raw_coef, class_code):
        gain = jnp.sum(jnp.where(classes == class_code[None], class_gain[:, None, None], 0.0), axis=0)
        return 0.2 * gain * raw_coef

    diffusivity = diffusion(cell_coef, jnp.broadcast_to(coef_class.astype(jnp.float32)[:, None], cell_coef.shape))
    state = jnp.concatenate([from_below[:-2], picked.astype(jnp.float32), from_above[:-2]], axis=1)
    coef_wide = jnp.concatenate(
        [diffusion(from_below[-2], from_below[-1]), diffusivity, diffusion(from_above[-2], from_above[-1])], axis=0
    )
    ext = lines + 2 * halo
    first = lax.axis_index("tile") * lines - halo
    line_no = first + lax.broadcasted_iota(jnp.int32, (ext, 1), 0)
    inside = (line_no >= 0) & (line_no < tiles * lines)
    coef_pad = jnp.pad(coef_wide, ((1, 1), (0, 0)))
    for sweep_no in range(SMOOTH):
        padded = jnp.pad(state, ((0, 0), (1, 1), (0, 0)))
        state = jnp.where(inside[None], step_core(padded, coef_pad), 0.0)
    state = state[:, halo : halo + lines]
    smoothed = state.astype(jnp.bfloat16).reshape(panel_count, per_block, lines, cells)
    flat_rows = adjoint_rows.reshape(resident, lines * cells)
    gram_scale = 1.0 / math.sqrt(tiles * lines * cells)
    rows_piece = lax.all_gather(smoothed, "rows", axis=1, tiled=True)
    panel = rows_piece.shape[1]
    flat_piece = rows_piece.reshape(-1, lines * cells)
    product = lax.dot_general(
        flat_piece, flat_rows, (((1,), (1,)), ((), ())), preferred_element_type=jnp.float32
    )
    terms = (product * gram_scale).reshape(panel_count, tiles, panel // tiles, resident)
    terms = terms.transpose(1, 0, 2, 3)
    parts = lax.all_to_all(terms, "tile", 0, 0, tiled=True)
    return jnp.sum(parts, axis=0)


def solution(mesh):
    return jax.shard_map(
        per_device,
        mesh=mesh,
        in_specs=(P("rows", "tile", None), P(None, "rows"), P("tile"), P(), P("tile", None)),
        out_specs=P(None, "tile", "rows"),
        check_vma=False,
    )
```

```python
import functools
import math

import jax
import jax.numpy as jnp
from jax import lax
from jax.experimental import pallas as pl
from jax.experimental.pallas import tpu as pltpu
from jax.sharding import PartitionSpec as P

SMOOTH = 4


def gather_kernel(halo, index_ref, class_ref, rows_ref, coef_ref, picked_ref, down_ref, up_ref, buf):
    panels, per_block = index_ref.shape
    count = panels * per_block
    lines = buf.shape[1]
    for i in range(count):
        buf[i] = rows_ref[index_ref[i // per_block, i % per_block]]
    picked_ref[...] = buf[...]
    rows = buf[...].astype(jnp.float32)
    code = jnp.full(down_ref.shape[1:], class_ref[0].astype(jnp.float32), jnp.float32)
    down_ref[:count] = rows[:, :halo]
    down_ref[count] = coef_ref[:halo]
    down_ref[count + 1] = code
    up_ref[:count] = rows[:, lines - halo :]
    up_ref[count] = coef_ref[lines - halo :]
    up_ref[count + 1] = code


def gather_rows(adjoint_rows, panel_index, coef_class, cell_coef, halo):
    count = panel_index.size
    lines, cells = cell_coef.shape
    edge = jax.ShapeDtypeStruct((count + 2, halo, cells), jnp.float32)
    smem = pl.BlockSpec(memory_space=pltpu.SMEM)
    vmem = pl.BlockSpec(memory_space=pltpu.VMEM)
    return pl.pallas_call(
        functools.partial(gather_kernel, halo),
        out_shape=(jax.ShapeDtypeStruct((count, lines, cells), adjoint_rows.dtype), edge, edge),
        in_specs=[smem, smem, vmem, vmem],
        out_specs=(vmem, vmem, vmem),
        scratch_shapes=[pltpu.VMEM((count, lines, cells), adjoint_rows.dtype)],
        cost_estimate=pl.CostEstimate(flops=0, transcendentals=0, bytes_accessed=count * lines * cells * 6),
    )(panel_index, coef_class, adjoint_rows, cell_coef)


def step_core(padded, coef_pad):
    middle = padded[..., 1:-1, :]
    coef_mid = coef_pad[1:-1, :]
    face_up = 0.5 * (coef_pad[:-2, :] + coef_mid)
    face_down = 0.5 * (coef_pad[2:, :] + coef_mid)
    side_vals = jnp.pad(middle, [(0, 0)] * (middle.ndim - 1) + [(1, 1)])
    side_coef = jnp.pad(coef_mid, ((0, 0), (1, 1)))
    face_left = 0.5 * (side_coef[:, :-2] + coef_mid)
    face_right = 0.5 * (side_coef[:, 2:] + coef_mid)
    result = middle + face_up * (padded[..., :-2, :] - middle)
    result = result + face_down * (padded[..., 2:, :] - middle)
    result = result + face_left * (side_vals[..., :-2] - middle)
    return result + face_right * (side_vals[..., 2:] - middle)


def per_device(adjoint_rows, panel_index, coef_class, class_gain, cell_coef):
    resident = adjoint_rows.shape[0]
    lines = cell_coef.shape[0]
    cells = cell_coef.shape[1]
    panel_count = panel_index.shape[0]
    per_block = panel_index.shape[1]
    tiles = lax.axis_size("tile")
    halo = SMOOTH
    assert lines >= halo
    picked, down_edge, up_edge = gather_rows(adjoint_rows, panel_index, coef_class, cell_coef, halo)
    count = lax.axis_size("tile")
    from_below = lax.ppermute(up_edge, "tile", [(i, i + 1) for i in range(count - 1)])
    from_above = lax.ppermute(down_edge, "tile", [(i + 1, i) for i in range(count - 1)])
    classes = lax.broadcasted_iota(jnp.int32, (class_gain.shape[0], 1, 1), 0).astype(jnp.float32)

    def diffusion(raw_coef, class_code):
        gain = jnp.sum(jnp.where(classes == class_code[None], class_gain[:, None, None], 0.0), axis=0)
        return 0.2 * gain * raw_coef

    diffusivity = diffusion(cell_coef, jnp.broadcast_to(coef_class.astype(jnp.float32)[:, None], cell_coef.shape))
    state = jnp.concatenate([from_below[:-2], picked.astype(jnp.float32), from_above[:-2]], axis=1)
    coef_wide = jnp.concatenate(
        [diffusion(from_below[-2], from_below[-1]), diffusivity, diffusion(from_above[-2], from_above[-1])], axis=0
    )
    ext = lines + 2 * halo
    first = lax.axis_index("tile") * lines - halo
    line_no = first + lax.broadcasted_iota(jnp.int32, (ext, 1), 0)
    inside = (line_no >= 0) & (line_no < tiles * lines)
    coef_pad = jnp.pad(coef_wide, ((1, 1), (0, 0)))
    for sweep_no in range(SMOOTH):
        padded = jnp.pad(state, ((0, 0), (1, 1), (0, 0)))
        state = jnp.where(inside[None], step_core(padded, coef_pad), 0.0)
    state = state[:, halo : halo + lines]
    smoothed = state.astype(jnp.bfloat16).reshape(panel_count, per_block, lines, cells)
    flat_rows = adjoint_rows.reshape(resident, lines * cells)
    gram_scale = 1.0 / math.sqrt(tiles * lines * cells)
    rows_piece = lax.all_gather(smoothed, "rows", axis=1, tiled=True)
    panel = rows_piece.shape[1]
    flat_piece = rows_piece.reshape(-1, lines * cells)
    product = lax.dot_general(
        flat_piece, flat_rows, (((1,), (1,)), ((), ())), preferred_element_type=jnp.float32
    )
    terms = (product * gram_scale).reshape(panel_count, tiles, panel // tiles, resident)
    terms = terms.transpose(1, 0, 2, 3)
    parts = lax.all_to_all(terms, "tile", 0, 0, tiled=True)
    return jnp.sum(parts, axis=0)


def solution(mesh):
    return jax.shard_map(
        per_device,
        mesh=mesh,
        in_specs=(P("rows", "tile", None), P(None, "rows"), P("tile"), P(), P("tile", None)),
        out_specs=P(None, "tile", "rows"),
        check_vma=False,
    )
```
